256 devices in a mesh: dp: 16 (over x, y_hi, core), mp: 16 (over y_lo, z).
Axes of the slice: x: 4, y: 4 (y_hi: 2, y_lo: 2; y = y_hi * 2 + y_lo), z: 8, core: 2. Of those that a mesh axis runs over, the one named last changes fastest.
Arguments:
- tokens: bfloat16 [4096, 4096], P('dp'), may hold values from -32 to 32
- weights: bfloat16 [4096, 2, 3, 4096], P('dp', None, None, 'mp'), may hold values from -1 to 1
- block_modality: int32 [32], replicated, may hold values from 0 to 1
- doc_ids: int32 [4096], replicated, may hold values from 0 to 31, never falling along the last dimension, each value on 1 to 1024 neighbouring positions
- grad_out: bfloat16 [4096, 4096], P('dp', 'mp'), may hold values from -6 to 6
Outputs:
- attended: bfloat16 [4096, 4096], P('dp', 'mp')
- grad_tokens: bfloat16 [4096, 4096], P('dp', 'mp')
- grad_weights: bfloat16 [4096, 2, 3, 4096], P('dp', None, None, 'mp')
The draws below stay inside these ranges and needn't reach their ends.
Inputs may be any that keep to these rules, and one draw needn't show every extreme that they name: doc_ids never falls along the sequence; a document is a run of equal ids of at most 1024 tokens, and one document has exactly 1024.
All inputs are finite; a program needn't handle non-finite values.
Results may differ from the reference program's by a relative error of at most 0.025.
Values may be sent and summed in bfloat16 or wider, within the bound.
No kernel may reach another device: no remote copies, remote signals or barrier semaphores. Data moves between devices by JAX's collectives and lax.ppermute only.
A program may use at most 128 MiB of HBM per device.

```python
import math
import jax
import jax.numpy as jnp
import numpy as np
from jax import lax

D = 4096
HEADS = 32
HD = 128
BLOCK = 128
SPAN = 4
TOK_DEV = 256
TOKENS = 4096
HQ = 4096
DOCS = 32
MAXDOC = 1024
N_DP = 16
N_MP = 16


def draw_tokens(key, part):
    own_key = jax.random.fold_in(key, 11)
    base_key = jax.random.fold_in(own_key, 0)
    base = jax.random.normal(base_key, (TOKENS, D), jnp.float32)
    return jnp.clip(base, -6.0, 6.0).astype(jnp.bfloat16)


def draw_weights(key, part):
    own_key = jax.random.fold_in(key, 23)
    single_key = jax.random.fold_in(own_key, 1)
    single = jax.random.normal(single_key, (D, 2, 3, HQ), jnp.float32)
    return (jnp.clip(single, -6.0, 6.0) * D ** (-0.5)).astype(jnp.bfloat16)


def plant(values, stream_key, low, top_value):
    extent = values.shape
    spot = [jax.random.randint(jax.random.fold_in(stream_key, axis), (), 0, extent[axis]) for axis in range(len(extent))]
    values = values.at[tuple(spot)].set(low)
    longest = extent.index(max(extent))
    spot[longest] = (spot[longest] + 1) % extent[longest]
    return values.at[tuple(spot)].set(top_value)


def level_of(rng, extent, pieces, smallest, largest):
    gain, own = 1.0, jax.random.fold_in(rng, 6)
    for dim, blocks in pieces:
        steps = jnp.exp(jax.random.uniform(jax.random.fold_in(own, dim), (blocks,), jnp.float32, smallest / len(pieces), largest / len(pieces)))
        gain = gain * jnp.repeat(steps, extent[dim] // blocks).reshape([-1 if axis == dim else 1 for axis in range(len(extent))])
    return gain


def profile(count, total, most, skew):
    portions = [(1 << 20) // math.isqrt(grade ** skew) + 1 for grade in range(2, count + 1)]
    spare, holding = total - most - (count - 1), [1] * (count - 1)
    while spare > 0:
        free = [i for i in range(count - 1) if holding[i] < most]
        mass, remaining = sum([portions[i] for i in free]), spare
        for i in free:
            addition = min(most - holding[i], max(1, remaining * portions[i] // mass), spare)
            holding[i] = holding[i] + addition
            spare = spare - addition
    return np.array([most] + holding)


def ragged(stream_key, count, total, limit, slope):
    if count == 2:
        one = jax.random.randint(stream_key, (), max(1, total - limit), min(limit, total - 1) + 1)
        return jnp.stack([one, total - one])
    sizes = jnp.asarray(profile(count, total, limit, slope), jnp.int32)
    twos = (count - 1) // 2
    source_of, taker = sizes[1:1 + 2 * twos:2], sizes[2:2 + 2 * twos:2]
    slack = jnp.minimum(source_of - 1, limit - taker)
    shifted = jax.random.randint(jax.random.fold_in(stream_key, 1), (twos,), 0, 1 << 20) % (slack + 1)
    sizes = sizes.at[1:1 + 2 * twos:2].set(source_of - shifted).at[2:2 + 2 * twos:2].set(taker + shifted)
    return sizes[jax.random.permutation(jax.random.fold_in(stream_key, 2), count)]


def gaussian(key, shape, scale, limit, cuts=(), kind=jnp.bfloat16):
    values = scale * jax.random.normal(key, shape, jnp.float32)
    if cuts:
        values = values * level_of(key, shape, cuts, -0.22, 0.18)
    return jnp.clip(values, -limit, limit).astype(kind)


def setup_inputs(seed: int = 0) -> dict:
    splits = jax.random.split(jax.random.key(seed), 6)
    return {
        "tokens": draw_tokens(jax.random.fold_in(splits[5], 71), 0),
        "weights": draw_weights(jax.random.fold_in(splits[5], 71), 0),
        "block_modality": plant(jax.random.randint(splits[2], (TOKENS // BLOCK,), 0, 2), jax.random.fold_in(splits[2], 1), 0, 1).astype(jnp.int32),
        "doc_ids": jnp.searchsorted(jnp.cumsum(ragged(splits[3], DOCS, TOKENS, MAXDOC, 2)), jnp.arange(TOKENS), side="right").astype(jnp.int32),
        "grad_out": gaussian(splits[4], (TOKENS, HQ), 1.0, 6.0, ((0, 16), (1, 16))),
    }


def reference(tokens, weights, block_modality, doc_ids, grad_out):
    scale_factor = HD ** -0.5
    block_count = TOKENS // BLOCK
    flat_weights = weights.reshape(D, 2, 3 * HQ)

    def project(pair):
        block_rows, modality = pair
        chosen = lax.dynamic_index_in_dim(flat_weights, modality, 1, keepdims=False)
        return jnp.dot(block_rows, chosen, preferred_element_type=jnp.float32).astype(jnp.bfloat16)

    qkv = lax.map(project, (tokens.reshape(block_count, BLOCK, D), block_modality))
    qkv = qkv.reshape(TOKENS, 3, HEADS, HD)
    queries = qkv[:, 0]
    front_pad = SPAN * TOK_DEV
    window_len = (SPAN + 1) * TOK_DEV
    zero_pad = jnp.zeros((front_pad, HEADS, HD), jnp.bfloat16)
    keys_pad = jnp.concatenate([zero_pad, qkv[:, 1]], 0)
    values_pad = jnp.concatenate([zero_pad, qkv[:, 2]], 0)
    docs_pad = jnp.concatenate([jnp.full((front_pad,), -1, jnp.int32), doc_ids], 0)
    upstream = grad_out.reshape(TOKENS, HEADS, HD)

    def one_block(accum, index):
        first_row = index * TOK_DEV
        query_rows = lax.dynamic_slice_in_dim(queries, first_row, TOK_DEV, 0).astype(jnp.float32)
        key_rows = lax.dynamic_slice_in_dim(keys_pad, first_row, window_len, 0).astype(jnp.float32)
        value_rows = lax.dynamic_slice_in_dim(values_pad, first_row, window_len, 0).astype(jnp.float32)
        query_docs = lax.dynamic_slice_in_dim(doc_ids, first_row, TOK_DEV, 0)
        key_docs = lax.dynamic_slice_in_dim(docs_pad, first_row, window_len, 0)
        offsets = jnp.arange(window_len, dtype=jnp.int32) - front_pad
        allowed = (key_docs[None, :] == query_docs[:, None]) & (offsets[None, :] <= jnp.arange(TOK_DEV, dtype=jnp.int32)[:, None])
        scores = jnp.einsum("qhd,khd->hqk", query_rows, key_rows) * scale_factor
        scores = jnp.where(allowed[None], scores, -1e30)
        top_score = jnp.max(scores, axis=-1, keepdims=True)
        expos = jnp.where(allowed[None], jnp.exp(scores - top_score), 0.0)
        probs_f = expos / jnp.sum(expos, axis=-1, keepdims=True)
        probs = probs_f.astype(jnp.bfloat16).astype(jnp.float32)
        result = jnp.einsum("hqk,khd->qhd", probs, value_rows).astype(jnp.bfloat16)
        grad_rows = lax.dynamic_slice_in_dim(upstream, first_row, TOK_DEV, 0).astype(jnp.float32)
        dprob = jnp.einsum("qhd,khd->hqk", grad_rows, value_rows)
        row_delta = jnp.sum(probs_f * dprob, axis=-1, keepdims=True)
        dscore = (probs_f * (dprob - row_delta)).astype(jnp.bfloat16).astype(jnp.float32)
        grad_q = jnp.einsum("hqk,khd->qhd", dscore, key_rows) * scale_factor
        grad_k = jnp.einsum("hqk,qhd->khd", dscore, query_rows) * scale_factor
        grad_v = jnp.einsum("hqk,qhd->khd", probs, grad_rows)
        window = lax.dynamic_slice_in_dim(accum, first_row, window_len, 0) + jnp.stack([grad_k, grad_v], 1)
        accum = lax.dynamic_update_slice_in_dim(accum, window, first_row, 0)
        return accum, (result, grad_q)

    accum_init = jnp.zeros((front_pad + TOKENS, 2, HEADS, HD), jnp.float32)
    accum, (results, grad_qs) = lax.scan(one_block, accum_init, jnp.arange(N_DP, dtype=jnp.int32))
    attended = results.reshape(TOKENS, HQ)
    grad_q_all = grad_qs.reshape(TOKENS, 1, HEADS, HD)
    grad_kv = accum[front_pad:]
    dqkv = jnp.concatenate([grad_q_all, grad_kv], 1).astype(jnp.bfloat16).reshape(TOKENS, 3 * HQ)

    token_mods = jnp.broadcast_to(block_modality[:, None], (block_count, BLOCK)).reshape(TOKENS)
    grad_list = []
    for modality in range(2):
        chosen_rows = jnp.where(token_mods[:, None] == modality, tokens, jnp.zeros_like(tokens))
        grad_list.append(lax.dot_general(chosen_rows, dqkv, (((0,), (0,)), ((), ())), preferred_element_type=jnp.float32))
    grad_weights = jnp.stack(grad_list, 1).astype(jnp.bfloat16).reshape(D, 2, 3, HQ)

    group_weights = weights.reshape(D, 2, 3, N_MP, HQ // N_MP)
    group_grads = dqkv.reshape(block_count, BLOCK, 3, N_MP, HQ // N_MP)

    def input_block(pair):
        block_grads, modality = pair
        chosen = lax.dynamic_index_in_dim(group_weights, modality, 1, keepdims=False).astype(jnp.float32)
        parts = jnp.einsum("nkjh,dkjh->jnd", block_grads.astype(jnp.float32), chosen)
        parts = parts.astype(jnp.bfloat16).astype(jnp.float32)
        return jnp.sum(parts, axis=0).astype(jnp.bfloat16)

    grad_tokens = lax.map(input_block, (group_grads, block_modality)).reshape(TOKENS, D)
    return attended, grad_tokens, grad_weights
```

```python
import jax
import jax.numpy as jnp
from jax import lax
from jax.sharding import PartitionSpec as P

HD = 128
BLOCK = 128
SPAN = 4


def shifted(block, axis, distance):
    devices = range(lax.axis_size(axis))
    route = [(i - distance, i) for i in devices if i - distance in devices]
    return lax.ppermute(block, axis, route)


def split_by_modality(rows, is_image):
    zeros = jnp.zeros_like(rows)
    text = jnp.where(is_image[:, None], zeros, rows)
    image = jnp.where(is_image[:, None], rows, zeros)
    return jnp.stack([text, image], axis=2).reshape(rows.shape[0], 2 * rows.shape[1])


def split_by_modality_major(rows, is_image):
    zeros = jnp.zeros_like(rows)
    text = jnp.where(is_image[:, None], zeros, rows)
    image = jnp.where(is_image[:, None], rows, zeros)
    return jnp.concatenate([text, image], axis=1)


def on_device(tokens, weights, block_modality, doc_ids, grad_out):
    local_rows = tokens.shape[0]
    width_rows = weights.shape[0]
    head_width = weights.shape[3]
    head_count = head_width // HD
    dp_devices = lax.axis_size("dp")
    mp_devices = lax.axis_size("mp")
    local_blocks = local_rows // BLOCK
    front_pad = SPAN * local_rows
    window_len = front_pad + local_rows
    my_index = lax.axis_index("dp")
    scale_factor = HD ** (-0.5)
    token_image = jnp.repeat(block_modality, BLOCK) == 1
    my_image = lax.dynamic_slice_in_dim(token_image, my_index * local_rows, local_rows, 0)

    flat_weights = weights.reshape(width_rows, 2, 3 * head_width)
    whole_weights = lax.all_gather(flat_weights, "dp", axis=0, tiled=True)
    columns = lax.all_to_all(tokens, "dp", split_axis=1, concat_axis=0, tiled=True)
    whole_weights, columns = lax.optimization_barrier((whole_weights, columns))
    stacked_weights = whole_weights.reshape(-1, 3 * head_width)

    summed = jnp.dot(
        split_by_modality(tokens, my_image), stacked_weights, preferred_element_type=jnp.float32
    )
    qkv = summed.astype(jnp.bfloat16).reshape(local_rows, 3, head_count, HD)
    queries = qkv[:, 0]
    key_values = qkv[:, 1:]
    received = []
    for distance in range(SPAN, 0, -1):
        received.append(shifted(key_values, "dp", distance))
    window = jnp.concatenate(received + [key_values], 0)
    key_rows = window[:, 0]
    value_rows = window[:, 1]
    docs_pad = jnp.concatenate([jnp.full((front_pad,), -1, jnp.int32), doc_ids], 0)
    key_docs = lax.dynamic_slice_in_dim(docs_pad, my_index * local_rows, window_len, 0)
    query_docs = lax.dynamic_slice_in_dim(doc_ids, my_index * local_rows, local_rows, 0)
    offsets = jnp.arange(window_len, dtype=jnp.int32) - front_pad
    allowed = (key_docs[None, :] == query_docs[:, None]) & (
        offsets[None, :] <= jnp.arange(local_rows, dtype=jnp.int32)[:, None]
    )
    scores = (
        jnp.einsum("qhd,khd->hqk", queries, key_rows, preferred_element_type=jnp.float32)
        * scale_factor
    )
    scores = jnp.where(allowed[None], scores, -1e30)
    top_score = jnp.max(scores, axis=-1, keepdims=True)
    expos = jnp.where(allowed[None], jnp.exp(scores - top_score), 0.0)
    probs_f = expos / jnp.sum(expos, axis=-1, keepdims=True)
    probs = probs_f.astype(jnp.bfloat16)
    attended = jnp.einsum("hqk,khd->qhd", probs, value_rows, preferred_element_type=jnp.float32)
    attended = attended.astype(jnp.bfloat16).reshape(local_rows, head_width)
    upstream = grad_out.reshape(local_rows, head_count, HD)
    dprob = jnp.einsum("qhd,khd->hqk", upstream, value_rows, preferred_element_type=jnp.float32)
    row_delta = jnp.sum(probs_f * dprob, axis=-1, keepdims=True)
    dscore = (probs_f * (dprob - row_delta)).astype(jnp.bfloat16)
    grad_q = (
        jnp.einsum("hqk,khd->qhd", dscore, key_rows, preferred_element_type=jnp.float32)
        * scale_factor
    )
    grad_k = (
        jnp.einsum("hqk,qhd->khd", dscore, queries, preferred_element_type=jnp.float32)
        * scale_factor
    )
    grad_v = jnp.einsum("hqk,qhd->khd", probs, upstream, preferred_element_type=jnp.float32)
    window_grads = jnp.stack([grad_k, grad_v], 1)
    own_grads = window_grads[front_pad:]
    for distance in range(1, SPAN + 1):
        lower_edge = front_pad - distance * local_rows
        sent_block = window_grads[lower_edge : lower_edge + local_rows]
        own_grads = own_grads + shifted(sent_block.astype(jnp.bfloat16), "dp", -distance).astype(
            sent_block.dtype
        )
    dqkv = (
        jnp.concatenate([grad_q[:, None], own_grads], 1)
        .astype(jnp.bfloat16)
        .reshape(local_rows, 3 * head_width)
    )

    parts = lax.dot_general(
        split_by_modality_major(dqkv, my_image),
        whole_weights.reshape(whole_weights.shape[0], -1),
        (((1,), (1,)), ((), ())),
        preferred_element_type=jnp.float32,
    ).astype(jnp.bfloat16)
    group_parts = lax.all_to_all(
        parts.reshape(local_rows, mp_devices, -1), "mp", split_axis=1, concat_axis=1, tiled=True
    )
    grad_tokens = jnp.sum(group_parts.astype(jnp.float32), axis=1).astype(jnp.bfloat16)

    gathered = lax.all_gather(dqkv, "dp", axis=0, tiled=True)
    weight_sum = lax.dot_general(
        columns,
        split_by_modality_major(gathered, token_image),
        (((0,), (0,)), ((), ())),
        preferred_element_type=jnp.float32,
    )
    grad_weights = weight_sum.astype(jnp.bfloat16).reshape(width_rows, 2, 3, head_width)
    return (attended, grad_tokens, grad_weights)


def solution(mesh):
    return jax.shard_map(
        on_device,
        mesh=mesh,
        in_specs=(P("dp", None), P("dp", None, None, "mp"), P(), P(), P("dp", "mp")),
        out_specs=(P("dp", "mp"), P("dp", "mp"), P("dp", None, None, "mp")),
        check_vma=False,
    )
```

```python
import jax
import jax.numpy as jnp
from jax import lax
from jax.sharding import PartitionSpec as P

HD = 128
BLOCK = 128
SPAN = 4


def shifted(block, axis, distance):
    devices = range(lax.axis_size(axis))
    route = [(i - distance, i) for i in devices if i - distance in devices]
    return lax.ppermute(block, axis, route)


def split_by_modality(rows, is_image):
    zeros = jnp.zeros_like(rows)
    text = jnp.where(is_image[:, None], zeros, rows)
    image = jnp.where(is_image[:, None], rows, zeros)
    return jnp.stack([text, image], axis=2).reshape(rows.shape[0], 2 * rows.shape[1])


def split_by_modality_major(rows, is_image):
    zeros = jnp.zeros_like(rows)
    text = jnp.where(is_image[:, None], zeros, rows)
    image = jnp.where(is_image[:, None], rows, zeros)
    return jnp.concatenate([text, image], axis=1)


def dp_ring(size):
    if size % 4:
        return list(range(size))
    chips = size // 2
    order = [2 * x for x in range(chips // 2)] + [2 * x + 1 for x in reversed(range(chips // 2))]
    return [2 * chip + core for chip in order for core in range(2)]


def ring_blocks(rows, ring, axis):
    shape = rows.shape
    blocks = rows.reshape(shape[:axis] + (len(ring), shape[axis] // len(ring)) + shape[axis + 1 :])
    return jnp.take(blocks, jnp.array(ring, jnp.int32), axis=axis).reshape(shape)


def on_device(tokens, weights, block_modality, doc_ids, grad_out):
    local_rows = tokens.shape[0]
    width_rows = weights.shape[0]
    head_width = weights.shape[3]
    head_count = head_width // HD
    dp_devices = lax.axis_size("dp")
    mp_devices = lax.axis_size("mp")
    local_blocks = local_rows // BLOCK
    front_pad = SPAN * local_rows
    window_len = front_pad + local_rows
    my_index = lax.axis_index("dp")
    scale_factor = HD ** (-0.5)
    token_image = jnp.repeat(block_modality, BLOCK) == 1
    my_image = lax.dynamic_slice_in_dim(token_image, my_index * local_rows, local_rows, 0)

    ring = dp_ring(dp_devices)
    inverse = [ring.index(k) for k in range(dp_devices)]
    flat_weights = weights.reshape(width_rows, 2, 3 * head_width)
    whole_weights = lax.all_gather(
        flat_weights, "dp", axis=0, tiled=True, axis_index_groups=[ring]
    )
    columns = lax.all_to_all(tokens, "dp", split_axis=1, concat_axis=0, tiled=True)
    ring_columns = split_by_modality_major(
        ring_blocks(columns, ring, 0), ring_blocks(token_image, ring, 0)
    )
    ring_tokens = split_by_modality(ring_blocks(tokens, ring, 1), my_image)
    whole_weights, ring_columns, ring_tokens = lax.optimization_barrier(
        (whole_weights, ring_columns, ring_tokens)
    )
    stacked_weights = whole_weights.reshape(-1, 3 * head_width)

    summed = jnp.dot(ring_tokens, stacked_weights, preferred_element_type=jnp.float32)
    qkv = summed.astype(jnp.bfloat16).reshape(local_rows, 3, head_count, HD)
    queries = qkv[:, 0]
    key_values = qkv[:, 1:]
    received = []
    for distance in range(SPAN, 0, -1):
        received.append(shifted(key_values, "dp", distance))
    window = jnp.concatenate(received + [key_values], 0)
    key_rows = window[:, 0]
    value_rows = window[:, 1]
    docs_pad = jnp.concatenate([jnp.full((front_pad,), -1, jnp.int32), doc_ids], 0)
    key_docs = lax.dynamic_slice_in_dim(docs_pad, my_index * local_rows, window_len, 0)
    query_docs = lax.dynamic_slice_in_dim(doc_ids, my_index * local_rows, local_rows, 0)
    offsets = jnp.arange(window_len, dtype=jnp.int32) - front_pad
    allowed = (key_docs[None, :] == query_docs[:, None]) & (
        offsets[None, :] <= jnp.arange(local_rows, dtype=jnp.int32)[:, None]
    )
    scores = (
        jnp.einsum("qhd,khd->hqk", queries, key_rows, preferred_element_type=jnp.float32)
        * scale_factor
    )
    scores = jnp.where(allowed[None], scores, -1e30)
    top_score = jnp.max(scores, axis=-1, keepdims=True)
    expos = jnp.where(allowed[None], jnp.exp(scores - top_score), 0.0)
    probs_f = expos / jnp.sum(expos, axis=-1, keepdims=True)
    probs = probs_f.astype(jnp.bfloat16)
    attended = jnp.einsum("hqk,khd->qhd", probs, value_rows, preferred_element_type=jnp.float32)
    attended = attended.astype(jnp.bfloat16).reshape(local_rows, head_width)
    upstream = grad_out.reshape(local_rows, head_count, HD)
    dprob = jnp.einsum("qhd,khd->hqk", upstream, value_rows, preferred_element_type=jnp.float32)
    row_delta = jnp.sum(probs_f * dprob, axis=-1, keepdims=True)
    dscore = (probs_f * (dprob - row_delta)).astype(jnp.bfloat16)
    grad_q = (
        jnp.einsum("hqk,khd->qhd", dscore, key_rows, preferred_element_type=jnp.float32)
        * scale_factor
    )
    grad_k = (
        jnp.einsum("hqk,qhd->khd", dscore, queries, preferred_element_type=jnp.float32)
        * scale_factor
    )
    grad_v = jnp.einsum("hqk,qhd->khd", probs, upstream, preferred_element_type=jnp.float32)
    window_grads = jnp.stack([grad_k, grad_v], 1)
    own_grads = window_grads[front_pad:]
    for distance in range(1, SPAN + 1):
        lower_edge = front_pad - distance * local_rows
        sent_block = window_grads[lower_edge : lower_edge + local_rows]
        own_grads = own_grads + shifted(sent_block.astype(jnp.bfloat16), "dp", -distance).astype(
            sent_block.dtype
        )
    dqkv = (
        jnp.concatenate([grad_q[:, None], own_grads], 1)
        .astype(jnp.bfloat16)
        .reshape(local_rows, 3 * head_width)
    )

    parts = lax.dot_general(
        split_by_modality_major(dqkv, my_image),
        whole_weights.reshape(whole_weights.shape[0], -1),
        (((1,), (1,)), ((), ())),
        preferred_element_type=jnp.float32,
    ).astype(jnp.bfloat16)
    parts = ring_blocks(parts, inverse, 1)
    group_parts = lax.all_to_all(
        parts.reshape(local_rows, mp_devices, -1), "mp", split_axis=1, concat_axis=1, tiled=True
    )
    grad_tokens = jnp.sum(group_parts.astype(jnp.float32), axis=1).astype(jnp.bfloat16)

    gathered = lax.all_gather(dqkv, "dp", axis=0, tiled=True, axis_index_groups=[ring])
    weight_sum = lax.dot_general(
        ring_columns,
        gathered,
        (((0,), (0,)), ((), ())),
        preferred_element_type=jnp.float32,
    )
    grad_weights = (
        weight_sum.astype(jnp.bfloat16)
        .reshape(2, width_rows, 3 * head_width)
        .transpose(1, 0, 2)
        .reshape(width_rows, 2, 3, head_width)
    )
    return (attended, grad_tokens, grad_weights)


def solution(mesh):
    return jax.shard_map(
        on_device,
        mesh=mesh,
        in_specs=(P("dp", None), P("dp", None, None, "mp"), P(), P(), P("dp", "mp")),
        out_specs=(P("dp", "mp"), P("dp", "mp"), P("dp", None, None, "mp")),
        check_vma=False,
    )
```

```python
import jax
import jax.numpy as jnp
from jax import lax
from jax.sharding import PartitionSpec as P

HD = 128
BLOCK = 128
SPAN = 4


def shifted(block, axis, distance):
    devices = range(lax.axis_size(axis))
    route = [(i - distance, i) for i in devices if i - distance in devices]
    return lax.ppermute(block, axis, route)


def split_by_modality(rows, is_image):
    zeros = jnp.zeros_like(rows)
    text = jnp.where(is_image[:, None], zeros, rows)
    image = jnp.where(is_image[:, None], rows, zeros)
    return jnp.stack([text, image], axis=2).reshape(rows.shape[0], 2 * rows.shape[1])


def split_by_modality_major(rows, is_image):
    zeros = jnp.zeros_like(rows)
    text = jnp.where(is_image[:, None], zeros, rows)
    image = jnp.where(is_image[:, None], rows, zeros)
    return jnp.concatenate([text, image], axis=1)


def dp_ring(size):
    if size % 4:
        return list(range(size))
    chips = size // 2
    order = [2 * x for x in range(chips // 2)] + [2 * x + 1 for x in reversed(range(chips // 2))]
    return [2 * chip + core for chip in order for core in range(2)]


def ring_blocks(rows, ring, axis):
    shape = rows.shape
    blocks = rows.reshape(shape[:axis] + (len(ring), shape[axis] // len(ring)) + shape[axis + 1 :])
    return jnp.take(blocks, jnp.array(ring, jnp.int32), axis=axis).reshape(shape)


def on_device(tokens, weights, block_modality, doc_ids, grad_out):
    local_rows = tokens.shape[0]
    width_rows = weights.shape[0]
    head_width = weights.shape[3]
    head_count = head_width // HD
    dp_devices = lax.axis_size("dp")
    mp_devices = lax.axis_size("mp")
    local_blocks = local_rows // BLOCK
    front_pad = SPAN * local_rows
    window_len = front_pad + local_rows
    my_index = lax.axis_index("dp")
    scale_factor = HD ** (-0.5)
    token_image = jnp.repeat(block_modality, BLOCK) == 1
    my_image = lax.dynamic_slice_in_dim(token_image, my_index * local_rows, local_rows, 0)

    ring = dp_ring(dp_devices)
    inverse = [ring.index(k) for k in range(dp_devices)]
    flat_weights = (
        weights.reshape(width_rows, 2, 3 * head_width)
        .transpose(1, 0, 2)
        .reshape(2 * width_rows, 3 * head_width)
    )
    stacked_weights = lax.all_gather(
        flat_weights, "dp", axis=0, tiled=True, axis_index_groups=[ring]
    )
    columns = lax.all_to_all(tokens, "dp", split_axis=1, concat_axis=0, tiled=True)
    ring_columns = split_by_modality_major(
        ring_blocks(columns, ring, 0), ring_blocks(token_image, ring, 0)
    )
    ring_tokens = ring_blocks(tokens, ring, 1).reshape(local_rows, dp_devices, 1, width_rows)
    ring_tokens = jnp.concatenate(
        [
            jnp.where(my_image[:, None, None, None], jnp.zeros_like(ring_tokens), ring_tokens),
            jnp.where(my_image[:, None, None, None], ring_tokens, jnp.zeros_like(ring_tokens)),
        ],
        axis=2,
    ).reshape(local_rows, -1)
    stacked_weights, ring_columns, ring_tokens = lax.optimization_barrier(
        (stacked_weights, ring_columns, ring_tokens)
    )
    block_weights = stacked_weights.reshape(dp_devices, 2, width_rows, 3 * head_width)

    summed = jnp.dot(ring_tokens, stacked_weights, preferred_element_type=jnp.float32)
    qkv = summed.astype(jnp.bfloat16).reshape(local_rows, 3, head_count, HD)
    queries = qkv[:, 0]
    key_values = qkv[:, 1:]
    received = []
    for distance in range(SPAN, 0, -1):
        received.append(shifted(key_values, "dp", distance))
    window = jnp.concatenate(received + [key_values], 0)
    key_rows = window[:, 0]
    value_rows = window[:, 1]
    docs_pad = jnp.concatenate([jnp.full((front_pad,), -1, jnp.int32), doc_ids], 0)
    key_docs = lax.dynamic_slice_in_dim(docs_pad, my_index * local_rows, window_len, 0)
    query_docs = lax.dynamic_slice_in_dim(doc_ids, my_index * local_rows, local_rows, 0)
    offsets = jnp.arange(window_len, dtype=jnp.int32) - front_pad
    allowed = (key_docs[None, :] == query_docs[:, None]) & (
        offsets[None, :] <= jnp.arange(local_rows, dtype=jnp.int32)[:, None]
    )
    scores = (
        jnp.einsum("qhd,khd->hqk", queries, key_rows, preferred_element_type=jnp.float32)
        * scale_factor
    )
    scores = jnp.where(allowed[None], scores, -1e30)
    top_score = jnp.max(scores, axis=-1, keepdims=True)
    expos = jnp.where(allowed[None], jnp.exp(scores - top_score), 0.0)
    probs_f = expos / jnp.sum(expos, axis=-1, keepdims=True)
    probs = probs_f.astype(jnp.bfloat16)
    attended = jnp.einsum("hqk,khd->qhd", probs, value_rows, preferred_element_type=jnp.float32)
    attended = attended.astype(jnp.bfloat16).reshape(local_rows, head_width)
    upstream = grad_out.reshape(local_rows, head_count, HD)
    dprob = jnp.einsum("qhd,khd->hqk", upstream, value_rows, preferred_element_type=jnp.float32)
    row_delta = jnp.sum(probs_f * dprob, axis=-1, keepdims=True)
    dscore = (probs_f * (dprob - row_delta)).astype(jnp.bfloat16)
    grad_q = (
        jnp.einsum("hqk,khd->qhd", dscore, key_rows, preferred_element_type=jnp.float32)
        * scale_factor
    )
    grad_k = (
        jnp.einsum("hqk,qhd->khd", dscore, queries, preferred_element_type=jnp.float32)
        * scale_factor
    )
    grad_v = jnp.einsum("hqk,qhd->khd", probs, upstream, preferred_element_type=jnp.float32)
    window_grads = jnp.stack([grad_k, grad_v], 1)
    own_grads = window_grads[front_pad:]
    for distance in range(1, SPAN + 1):
        lower_edge = front_pad - distance * local_rows
        sent_block = window_grads[lower_edge : lower_edge + local_rows]
        own_grads = own_grads + shifted(sent_block.astype(jnp.bfloat16), "dp", -distance).astype(
            sent_block.dtype
        )
    dqkv = (
        jnp.concatenate([grad_q[:, None], own_grads], 1)
        .astype(jnp.bfloat16)
        .reshape(local_rows, 3 * head_width)
    )

    zeros = jnp.zeros_like(dqkv)
    parts = lax.dot_general(
        jnp.where(my_image[:, None], zeros, dqkv),
        block_weights[:, 0],
        (((1,), (2,)), ((), ())),
        preferred_element_type=jnp.float32,
    ) + lax.dot_general(
        jnp.where(my_image[:, None], dqkv, zeros),
        block_weights[:, 1],
        (((1,), (2,)), ((), ())),
        preferred_element_type=jnp.float32,
    )
    parts = ring_blocks(parts.astype(jnp.bfloat16).reshape(local_rows, -1), inverse, 1)
    group_parts = lax.all_to_all(
        parts.reshape(local_rows, mp_devices, -1), "mp", split_axis=1, concat_axis=1, tiled=True
    )
    grad_tokens = jnp.sum(group_parts.astype(jnp.float32), axis=1).astype(jnp.bfloat16)

    gathered = lax.all_gather(dqkv, "dp", axis=0, tiled=True, axis_index_groups=[ring])
    weight_sum = lax.dot_general(
        ring_columns,
        gathered,
        (((0,), (0,)), ((), ())),
        preferred_element_type=jnp.float32,
    )
    grad_weights = (
        weight_sum.astype(jnp.bfloat16)
        .reshape(2, width_rows, 3 * head_width)
        .transpose(1, 0, 2)
        .reshape(width_rows, 2, 3, head_width)
    )
    return (attended, grad_tokens, grad_weights)


def solution(mesh):
    return jax.shard_map(
        on_device,
        mesh=mesh,
        in_specs=(P("dp", None), P("dp", None, None, "mp"), P(), P(), P("dp", "mp")),
        out_specs=(P("dp", "mp"), P("dp", "mp"), P("dp", None, None, "mp")),
        check_vma=False,
    )
```

```python
import jax
import jax.numpy as jnp
from jax import lax
from jax.sharding import PartitionSpec as P

HD = 128
BLOCK = 128
SPAN = 4


def shifted(block, axis, distance):
    devices = range(lax.axis_size(axis))
    route = [(i - distance, i) for i in devices if i - distance in devices]
    return lax.ppermute(block, axis, route)


def split_by_modality(rows, is_image):
    zeros = jnp.zeros_like(rows)
    text = jnp.where(is_image[:, None], zeros, rows)
    image = jnp.where(is_image[:, None], rows, zeros)
    return jnp.stack([text, image], axis=2).reshape(rows.shape[0], 2 * rows.shape[1])


def split_by_modality_major(rows, is_image):
    zeros = jnp.zeros_like(rows)
    text = jnp.where(is_image[:, None], zeros, rows)
    image = jnp.where(is_image[:, None], rows, zeros)
    return jnp.concatenate([text, image], axis=1)


def dp_ring(size):
    if size % 4:
        return list(range(size))
    chips = size // 2
    order = [2 * x for x in range(chips // 2)] + [2 * x + 1 for x in reversed(range(chips // 2))]
    return [2 * chip + core for chip in order for core in range(2)]


def ring_blocks(rows, ring, axis):
    shape = rows.shape
    blocks = rows.reshape(shape[:axis] + (len(ring), shape[axis] // len(ring)) + shape[axis + 1 :])
    return jnp.take(blocks, jnp.array(ring, jnp.int32), axis=axis).reshape(shape)


def on_device(tokens, weights, block_modality, doc_ids, grad_out):
    local_rows = tokens.shape[0]
    width_rows = weights.shape[0]
    head_width = weights.shape[3]
    head_count = head_width // HD
    dp_devices = lax.axis_size("dp")
    mp_devices = lax.axis_size("mp")
    local_blocks = local_rows // BLOCK
    front_pad = SPAN * local_rows
    window_len = front_pad + local_rows
    my_index = lax.axis_index("dp")
    scale_factor = HD ** (-0.5)
    token_image = jnp.repeat(block_modality, BLOCK) == 1
    my_image = lax.dynamic_slice_in_dim(token_image, my_index * local_rows, local_rows, 0)

    ring = dp_ring(dp_devices)
    inverse = [ring.index(k) for k in range(dp_devices)]
    flat_weights = (
        weights.reshape(width_rows, 2, 3 * head_width)
        .transpose(1, 0, 2)
        .reshape(2 * width_rows, 3 * head_width)
    )
    stacked_weights = lax.all_gather(
        flat_weights, "dp", axis=0, tiled=True, axis_index_groups=[ring]
    )
    columns = lax.all_to_all(tokens, "dp", split_axis=1, concat_axis=0, tiled=True)
    ring_columns = split_by_modality_major(
        ring_blocks(columns, ring, 0), ring_blocks(token_image, ring, 0)
    )
    ring_tokens = ring_blocks(tokens, ring, 1).reshape(local_rows, dp_devices, 1, width_rows)
    ring_tokens = jnp.concatenate(
        [
            jnp.where(my_image[:, None, None, None], jnp.zeros_like(ring_tokens), ring_tokens),
            jnp.where(my_image[:, None, None, None], ring_tokens, jnp.zeros_like(ring_tokens)),
        ],
        axis=2,
    ).reshape(local_rows, -1)
    stacked_weights, ring_columns, ring_tokens = lax.optimization_barrier(
        (stacked_weights, ring_columns, ring_tokens)
    )
    block_weights = stacked_weights.reshape(dp_devices, 2, width_rows, 3 * head_width)

    key_values = (
        jnp.dot(ring_tokens, stacked_weights[:, head_width:], preferred_element_type=jnp.float32)
        .astype(jnp.bfloat16)
        .reshape(local_rows, 2, head_count, HD)
    )
    received = []
    for distance in range(SPAN, 0, -1):
        received.append(shifted(key_values, "dp", distance))
    queries = (
        jnp.dot(ring_tokens, stacked_weights[:, :head_width], preferred_element_type=jnp.float32)
        .astype(jnp.bfloat16)
        .reshape(local_rows, head_count, HD)
    )
    window = jnp.concatenate(received + [key_values], 0)
    key_rows = window[:, 0]
    value_rows = window[:, 1]
    docs_pad = jnp.concatenate([jnp.full((front_pad,), -1, jnp.int32), doc_ids], 0)
    key_docs = lax.dynamic_slice_in_dim(docs_pad, my_index * local_rows, window_len, 0)
    query_docs = lax.dynamic_slice_in_dim(doc_ids, my_index * local_rows, local_rows, 0)
    offsets = jnp.arange(window_len, dtype=jnp.int32) - front_pad
    allowed = (key_docs[None, :] == query_docs[:, None]) & (
        offsets[None, :] <= jnp.arange(local_rows, dtype=jnp.int32)[:, None]
    )
    scores = (
        jnp.einsum("qhd,khd->hqk", queries, key_rows, preferred_element_type=jnp.float32)
        * scale_factor
    )
    scores = jnp.where(allowed[None], scores, -1e30)
    top_score = jnp.max(scores, axis=-1, keepdims=True)
    expos = jnp.where(allowed[None], jnp.exp(scores - top_score), 0.0)
    probs_f = expos / jnp.sum(expos, axis=-1, keepdims=True)
    probs = probs_f.astype(jnp.bfloat16)
    attended = jnp.einsum("hqk,khd->qhd", probs, value_rows, preferred_element_type=jnp.float32)
    attended = attended.astype(jnp.bfloat16).reshape(local_rows, head_width)
    upstream = grad_out.reshape(local_rows, head_count, HD)
    dprob = jnp.einsum("qhd,khd->hqk", upstream, value_rows, preferred_element_type=jnp.float32)
    row_delta = jnp.sum(probs_f * dprob, axis=-1, keepdims=True)
    dscore = (probs_f * (dprob - row_delta)).astype(jnp.bfloat16)
    grad_q = (
        jnp.einsum("hqk,khd->qhd", dscore, key_rows, preferred_element_type=jnp.float32)
        * scale_factor
    )
    grad_k = (
        jnp.einsum("hqk,qhd->khd", dscore, queries, preferred_element_type=jnp.float32)
        * scale_factor
    )
    grad_v = jnp.einsum("hqk,qhd->khd", probs, upstream, preferred_element_type=jnp.float32)
    window_grads = jnp.stack([grad_k, grad_v], 1)
    own_grads = window_grads[front_pad:]
    for distance in range(1, SPAN + 1):
        lower_edge = front_pad - distance * local_rows
        sent_block = window_grads[lower_edge : lower_edge + local_rows]
        own_grads = own_grads + shifted(sent_block.astype(jnp.bfloat16), "dp", -distance).astype(
            sent_block.dtype
        )
    dqkv = (
        jnp.concatenate([grad_q[:, None], own_grads], 1)
        .astype(jnp.bfloat16)
        .reshape(local_rows, 3 * head_width)
    )

    zeros = jnp.zeros_like(dqkv)
    parts = lax.dot_general(
        jnp.where(my_image[:, None], zeros, dqkv),
        block_weights[:, 0],
        (((1,), (2,)), ((), ())),
        preferred_element_type=jnp.float32,
    ) + lax.dot_general(
        jnp.where(my_image[:, None], dqkv, zeros),
        block_weights[:, 1],
        (((1,), (2,)), ((), ())),
        preferred_element_type=jnp.float32,
    )
    parts = ring_blocks(parts.astype(jnp.bfloat16).reshape(local_rows, -1), inverse, 1)
    group_parts = lax.all_to_all(
        parts.reshape(local_rows, mp_devices, -1), "mp", split_axis=1, concat_axis=1, tiled=True
    )
    grad_tokens = jnp.sum(group_parts.astype(jnp.float32), axis=1).astype(jnp.bfloat16)

    gathered = lax.all_gather(dqkv, "dp", axis=0, tiled=True, axis_index_groups=[ring])
    weight_sum = lax.dot_general(
        ring_columns,
        gathered,
        (((0,), (0,)), ((), ())),
        preferred_element_type=jnp.float32,
    )
    grad_weights = (
        weight_sum.astype(jnp.bfloat16)
        .reshape(2, width_rows, 3 * head_width)
        .transpose(1, 0, 2)
        .reshape(width_rows, 2, 3, head_width)
    )
    return (attended, grad_tokens, grad_weights)


def solution(mesh):
    return jax.shard_map(
        on_device,
        mesh=mesh,
        in_specs=(P("dp", None), P("dp", None, None, "mp"), P(), P(), P("dp", "mp")),
        out_specs=(P("dp", "mp"), P("dp", "mp"), P("dp", None, None, "mp")),
        check_vma=False,
    )
```

```python
import jax
import jax.numpy as jnp
from jax import lax
from jax.sharding import PartitionSpec as P

HD = 128
BLOCK = 128
SPAN = 4


def shifted(block, axis, distance):
    devices = range(lax.axis_size(axis))
    route = [(i - distance, i) for i in devices if i - distance in devices]
    return lax.ppermute(block, axis, route)


def split_by_modality(rows, is_image):
    zeros = jnp.zeros_like(rows)
    text = jnp.where(is_image[:, None], zeros, rows)
    image = jnp.where(is_image[:, None], rows, zeros)
    return jnp.stack([text, image], axis=2).reshape(rows.shape[0], 2 * rows.shape[1])


def split_by_modality_major(rows, is_image):
    zeros = jnp.zeros_like(rows)
    text = jnp.where(is_image[:, None], zeros, rows)
    image = jnp.where(is_image[:, None], rows, zeros)
    return jnp.concatenate([text, image], axis=1)


def dp_ring(size):
    if size % 4:
        return list(range(size))
    chips = size // 2
    order = [2 * x for x in range(chips // 2)] + [2 * x + 1 for x in reversed(range(chips // 2))]
    return [2 * chip + core for chip in order for core in range(2)]


def ring_blocks(rows, ring, axis):
    shape = rows.shape
    blocks = rows.reshape(shape[:axis] + (len(ring), shape[axis] // len(ring)) + shape[axis + 1 :])
    return jnp.take(blocks, jnp.array(ring, jnp.int32), axis=axis).reshape(shape)


def on_device(tokens, weights, block_modality, doc_ids, grad_out):
    local_rows = tokens.shape[0]
    width_rows = weights.shape[0]
    head_width = weights.shape[3]
    head_count = head_width // HD
    dp_devices = lax.axis_size("dp")
    mp_devices = lax.axis_size("mp")
    local_blocks = local_rows // BLOCK
    front_pad = SPAN * local_rows
    window_len = front_pad + local_rows
    my_index = lax.axis_index("dp")
    scale_factor = HD ** (-0.5)
    token_image = jnp.repeat(block_modality, BLOCK) == 1
    my_image = lax.dynamic_slice_in_dim(token_image, my_index * local_rows, local_rows, 0)

    ring = dp_ring(dp_devices)
    inverse = [ring.index(k) for k in range(dp_devices)]
    flat_weights = (
        weights.reshape(width_rows, 2, 3 * head_width)
        .transpose(1, 0, 2)
        .reshape(2 * width_rows, 3 * head_width)
    )
    stacked_weights = lax.all_gather(
        flat_weights, "dp", axis=0, tiled=True, axis_index_groups=[ring]
    )
    columns = lax.all_to_all(tokens, "dp", split_axis=1, concat_axis=0, tiled=True)
    ring_columns = split_by_modality_major(
        ring_blocks(columns, ring, 0), ring_blocks(token_image, ring, 0)
    )
    ring_tokens = ring_blocks(tokens, ring, 1).reshape(local_rows, dp_devices, 1, width_rows)
    ring_tokens = jnp.concatenate(
        [
            jnp.where(my_image[:, None, None, None], jnp.zeros_like(ring_tokens), ring_tokens),
            jnp.where(my_image[:, None, None, None], ring_tokens, jnp.zeros_like(ring_tokens)),
        ],
        axis=2,
    ).reshape(local_rows, -1)
    stacked_weights, ring_columns, ring_tokens = lax.optimization_barrier(
        (stacked_weights, ring_columns, ring_tokens)
    )
    block_weights = stacked_weights.reshape(dp_devices, 2, width_rows, 3 * head_width)

    key_values = (
        jnp.dot(ring_tokens, stacked_weights[:, head_width:], preferred_element_type=jnp.float32)
        .astype(jnp.bfloat16)
        .reshape(local_rows, 2, head_count, HD)
    )
    received = []
    for distance in range(SPAN, 0, -1):
        received.append(shifted(key_values, "dp", distance))
    queries = (
        jnp.dot(ring_tokens, stacked_weights[:, :head_width], preferred_element_type=jnp.float32)
        .astype(jnp.bfloat16)
        .reshape(local_rows, head_count, HD)
    )
    window = jnp.concatenate(received + [key_values], 0)
    key_rows = window[:, 0]
    value_rows = window[:, 1]
    docs_pad = jnp.concatenate([jnp.full((front_pad,), -1, jnp.int32), doc_ids], 0)
    key_docs = lax.dynamic_slice_in_dim(docs_pad, my_index * local_rows, window_len, 0)
    query_docs = lax.dynamic_slice_in_dim(doc_ids, my_index * local_rows, local_rows, 0)
    offsets = jnp.arange(window_len, dtype=jnp.int32) - front_pad
    allowed = (key_docs[None, :] == query_docs[:, None]) & (
        offsets[None, :] <= jnp.arange(local_rows, dtype=jnp.int32)[:, None]
    )
    scores = (
        jnp.einsum("qhd,khd->hqk", queries, key_rows, preferred_element_type=jnp.float32)
        * scale_factor
    )
    scores = jnp.where(allowed[None], scores, -1e30)
    top_score = jnp.max(scores, axis=-1, keepdims=True)
    expos = jnp.where(allowed[None], jnp.exp(scores - top_score), 0.0)
    probs_f = expos / jnp.sum(expos, axis=-1, keepdims=True)
    probs = probs_f.astype(jnp.bfloat16)
    attended = jnp.einsum("hqk,khd->qhd", probs, value_rows, preferred_element_type=jnp.float32)
    attended = attended.astype(jnp.bfloat16).reshape(local_rows, head_width)
    upstream = grad_out.reshape(local_rows, head_count, HD)
    dprob = jnp.einsum("qhd,khd->hqk", upstream, value_rows, preferred_element_type=jnp.float32)
    row_delta = jnp.sum(probs_f * dprob, axis=-1, keepdims=True)
    dscore = (probs_f * (dprob - row_delta)).astype(jnp.bfloat16)
    grad_q = (
        jnp.einsum("hqk,khd->qhd", dscore, key_rows, preferred_element_type=jnp.float32)
        * scale_factor
    )
    grad_k = (
        jnp.einsum("hqk,qhd->khd", dscore, queries, preferred_element_type=jnp.float32)
        * scale_factor
    )
    grad_v = jnp.einsum("hqk,qhd->khd", probs, upstream, preferred_element_type=jnp.float32)
    window_grads = jnp.stack([grad_k, grad_v], 1)
    own_grads = window_grads[front_pad:]
    for distance in range(1, SPAN + 1):
        lower_edge = front_pad - distance * local_rows
        sent_block = window_grads[lower_edge : lower_edge + local_rows]
        own_grads = own_grads + shifted(sent_block.astype(jnp.bfloat16), "dp", -distance).astype(
            sent_block.dtype
        )
    dqkv = (
        jnp.concatenate([grad_q[:, None], own_grads], 1)
        .astype(jnp.bfloat16)
        .reshape(local_rows, 3 * head_width)
    )

    zeros = jnp.zeros_like(dqkv)
    parts = lax.dot_general(
        jnp.where(my_image[:, None], zeros, dqkv),
        block_weights[:, 0],
        (((1,), (2,)), ((), ())),
        preferred_element_type=jnp.float32,
    ) + lax.dot_general(
        jnp.where(my_image[:, None], dqkv, zeros),
        block_weights[:, 1],
        (((1,), (2,)), ((), ())),
        preferred_element_type=jnp.float32,
    )
    parts = jnp.take(
        parts.astype(jnp.bfloat16).transpose(1, 0, 2), jnp.array(inverse, jnp.int32), axis=0
    ).reshape(mp_devices, local_rows, -1)
    group_parts = lax.all_to_all(parts, "mp", split_axis=0, concat_axis=0, tiled=True)
    grad_tokens = jnp.sum(group_parts.astype(jnp.float32), axis=0).astype(jnp.bfloat16)

    gathered = lax.all_gather(dqkv, "dp", axis=0, tiled=True, axis_index_groups=[ring])
    weight_sum = lax.dot_general(
        ring_columns,
        gathered,
        (((0,), (0,)), ((), ())),
        preferred_element_type=jnp.float32,
    )
    grad_weights = (
        weight_sum.astype(jnp.bfloat16)
        .reshape(2, width_rows, 3 * head_width)
        .transpose(1, 0, 2)
        .reshape(width_rows, 2, 3, head_width)
    )
    return (attended, grad_tokens, grad_weights)


def solution(mesh):
    return jax.shard_map(
        on_device,
        mesh=mesh,
        in_specs=(P("dp", None), P("dp", None, None, "mp"), P(), P(), P("dp", "mp")),
        out_specs=(P("dp", "mp"), P("dp", "mp"), P("dp", None, None, "mp")),
        check_vma=False,
    )
```

```python
import jax
import jax.numpy as jnp
from jax import lax
from jax.sharding import PartitionSpec as P

HD = 128
BLOCK = 128
SPAN = 4


def shifted(block, axis, distance):
    devices = range(lax.axis_size(axis))
    route = [(i - distance, i) for i in devices if i - distance in devices]
    return lax.ppermute(block, axis, route)


def split_by_modality(rows, is_image):
    zeros = jnp.zeros_like(rows)
    text = jnp.where(is_image[:, None], zeros, rows)
    image = jnp.where(is_image[:, None], rows, zeros)
    return jnp.stack([text, image], axis=2).reshape(rows.shape[0], 2 * rows.shape[1])


def split_by_modality_major(rows, is_image):
    zeros = jnp.zeros_like(rows)
    text = jnp.where(is_image[:, None], zeros, rows)
    image = jnp.where(is_image[:, None], rows, zeros)
    return jnp.concatenate([text, image], axis=1)


def dp_ring(size):
    if size % 4:
        return list(range(size))
    chips = size // 2
    order = [2 * x for x in range(chips // 2)] + [2 * x + 1 for x in reversed(range(chips // 2))]
    return [2 * chip + core for chip in order for core in range(2)]


def ring_blocks(rows, ring, axis):
    shape = rows.shape
    blocks = rows.reshape(shape[:axis] + (len(ring), shape[axis] // len(ring)) + shape[axis + 1 :])
    return jnp.take(blocks, jnp.array(ring, jnp.int32), axis=axis).reshape(shape)


def on_device(tokens, weights, block_modality, doc_ids, grad_out):
    local_rows = tokens.shape[0]
    width_rows = weights.shape[0]
    head_width = weights.shape[3]
    head_count = head_width // HD
    dp_devices = lax.axis_size("dp")
    mp_devices = lax.axis_size("mp")
    local_blocks = local_rows // BLOCK
    front_pad = SPAN * local_rows
    window_len = front_pad + local_rows
    my_index = lax.axis_index("dp")
    scale_factor = HD ** (-0.5)
    token_image = jnp.repeat(block_modality, BLOCK) == 1
    my_image = lax.dynamic_slice_in_dim(token_image, my_index * local_rows, local_rows, 0)

    ring = dp_ring(dp_devices)
    inverse = [ring.index(k) for k in range(dp_devices)]
    flat_weights = (
        weights.reshape(width_rows, 2, 3 * head_width)
        .transpose(1, 0, 2)
        .reshape(2 * width_rows, 3 * head_width)
    )
    stacked_weights = lax.all_gather(
        flat_weights, "dp", axis=0, tiled=True, axis_index_groups=[ring]
    )
    columns = lax.all_to_all(tokens, "dp", split_axis=1, concat_axis=0, tiled=True)
    ring_columns = split_by_modality_major(
        ring_blocks(columns, ring, 0), ring_blocks(token_image, ring, 0)
    )
    ring_tokens = ring_blocks(tokens, ring, 1).reshape(local_rows, dp_devices, 1, width_rows)
    ring_tokens = jnp.concatenate(
        [
            jnp.where(my_image[:, None, None, None], jnp.zeros_like(ring_tokens), ring_tokens),
            jnp.where(my_image[:, None, None, None], ring_tokens, jnp.zeros_like(ring_tokens)),
        ],
        axis=2,
    ).reshape(local_rows, -1)
    stacked_weights, ring_columns, ring_tokens = lax.optimization_barrier(
        (stacked_weights, ring_columns, ring_tokens)
    )
    block_weights = stacked_weights.reshape(dp_devices, 2, width_rows, 3 * head_width)

    key_values = (
        jnp.dot(ring_tokens, stacked_weights[:, head_width:], preferred_element_type=jnp.float32)
        .astype(jnp.bfloat16)
        .reshape(local_rows, 2, head_count, HD)
    )
    queries = (
        jnp.dot(ring_tokens, stacked_weights[:, :head_width], preferred_element_type=jnp.float32)
        .astype(jnp.bfloat16)
        .reshape(local_rows, head_count, HD)
    )
    sent_values, queries = lax.optimization_barrier((key_values, queries))
    received = []
    for distance in range(SPAN, 0, -1):
        received.append(shifted(sent_values, "dp", distance))
    window = jnp.concatenate(received + [key_values], 0)
    key_rows = window[:, 0]
    value_rows = window[:, 1]
    docs_pad = jnp.concatenate([jnp.full((front_pad,), -1, jnp.int32), doc_ids], 0)
    key_docs = lax.dynamic_slice_in_dim(docs_pad, my_index * local_rows, window_len, 0)
    query_docs = lax.dynamic_slice_in_dim(doc_ids, my_index * local_rows, local_rows, 0)
    offsets = jnp.arange(window_len, dtype=jnp.int32) - front_pad
    allowed = (key_docs[None, :] == query_docs[:, None]) & (
        offsets[None, :] <= jnp.arange(local_rows, dtype=jnp.int32)[:, None]
    )
    scores = (
        jnp.einsum("qhd,khd->hqk", queries, key_rows, preferred_element_type=jnp.float32)
        * scale_factor
    )
    scores = jnp.where(allowed[None], scores, -1e30)
    top_score = jnp.max(scores, axis=-1, keepdims=True)
    expos = jnp.where(allowed[None], jnp.exp(scores - top_score), 0.0)
    probs_f = expos / jnp.sum(expos, axis=-1, keepdims=True)
    probs = probs_f.astype(jnp.bfloat16)
    attended = jnp.einsum("hqk,khd->qhd", probs, value_rows, preferred_element_type=jnp.float32)
    attended = attended.astype(jnp.bfloat16).reshape(local_rows, head_width)
    upstream = grad_out.reshape(local_rows, head_count, HD)
    dprob = jnp.einsum("qhd,khd->hqk", upstream, value_rows, preferred_element_type=jnp.float32)
    row_delta = jnp.sum(probs_f * dprob, axis=-1, keepdims=True)
    dscore = (probs_f * (dprob - row_delta)).astype(jnp.bfloat16)
    grad_q = (
        jnp.einsum("hqk,khd->qhd", dscore, key_rows, preferred_element_type=jnp.float32)
        * scale_factor
    )
    grad_k = (
        jnp.einsum("hqk,qhd->khd", dscore, queries, preferred_element_type=jnp.float32)
        * scale_factor
    )
    grad_v = jnp.einsum("hqk,qhd->khd", probs, upstream, preferred_element_type=jnp.float32)
    window_grads = jnp.stack([grad_k, grad_v], 1)
    own_grads = window_grads[front_pad:]
    for distance in range(1, SPAN + 1):
        lower_edge = front_pad - distance * local_rows
        sent_block = window_grads[lower_edge : lower_edge + local_rows]
        own_grads = own_grads + shifted(sent_block.astype(jnp.bfloat16), "dp", -distance).astype(
            sent_block.dtype
        )
    dqkv = (
        jnp.concatenate([grad_q[:, None], own_grads], 1)
        .astype(jnp.bfloat16)
        .reshape(local_rows, 3 * head_width)
    )

    zeros = jnp.zeros_like(dqkv)
    parts = lax.dot_general(
        jnp.where(my_image[:, None], zeros, dqkv),
        block_weights[:, 0],
        (((1,), (2,)), ((), ())),
        preferred_element_type=jnp.float32,
    ) + lax.dot_general(
        jnp.where(my_image[:, None], dqkv, zeros),
        block_weights[:, 1],
        (((1,), (2,)), ((), ())),
        preferred_element_type=jnp.float32,
    )
    parts = jnp.take(
        parts.astype(jnp.bfloat16).transpose(1, 0, 2), jnp.array(inverse, jnp.int32), axis=0
    ).reshape(mp_devices, local_rows, -1)
    group_parts = lax.all_to_all(parts, "mp", split_axis=0, concat_axis=0, tiled=True)
    grad_tokens = jnp.sum(group_parts.astype(jnp.float32), axis=0).astype(jnp.bfloat16)

    gathered = lax.all_gather(dqkv, "dp", axis=0, tiled=True, axis_index_groups=[ring])
    weight_sum = lax.dot_general(
        ring_columns,
        gathered,
        (((0,), (0,)), ((), ())),
        preferred_element_type=jnp.float32,
    )
    grad_weights = (
        weight_sum.astype(jnp.bfloat16)
        .reshape(2, width_rows, 3 * head_width)
        .transpose(1, 0, 2)
        .reshape(width_rows, 2, 3, head_width)
    )
    return (attended, grad_tokens, grad_weights)


def solution(mesh):
    return jax.shard_map(
        on_device,
        mesh=mesh,
        in_specs=(P("dp", None), P("dp", None, None, "mp"), P(), P(), P("dp", "mp")),
        out_specs=(P("dp", "mp"), P("dp", "mp"), P("dp", None, None, "mp")),
        check_vma=False,
    )
```

```python
import jax
import jax.numpy as jnp
from jax import lax
from jax.sharding import PartitionSpec as P

HD = 128
BLOCK = 128
SPAN = 4


def shifted(block, axis, distance):
    devices = range(lax.axis_size(axis))
    route = [(i - distance, i) for i in devices if i - distance in devices]
    return lax.ppermute(block, axis, route)


def split_by_modality(rows, is_image):
    zeros = jnp.zeros_like(rows)
    text = jnp.where(is_image[:, None], zeros, rows)
    image = jnp.where(is_image[:, None], rows, zeros)
    return jnp.stack([text, image], axis=2).reshape(rows.shape[0], 2 * rows.shape[1])


def split_by_modality_major(rows, is_image):
    zeros = jnp.zeros_like(rows)
    text = jnp.where(is_image[:, None], zeros, rows)
    image = jnp.where(is_image[:, None], rows, zeros)
    return jnp.concatenate([text, image], axis=1)


def dp_ring(size):
    if size % 4:
        return list(range(size))
    chips = size // 2
    order = [2 * x for x in range(chips // 2)] + [2 * x + 1 for x in reversed(range(chips // 2))]
    return [2 * chip + core for chip in order for core in range(2)]


def ring_blocks(rows, ring, axis):
    shape = rows.shape
    blocks = rows.reshape(shape[:axis] + (len(ring), shape[axis] // len(ring)) + shape[axis + 1 :])
    return jnp.take(blocks, jnp.array(ring, jnp.int32), axis=axis).reshape(shape)


def on_device(tokens, weights, block_modality, doc_ids, grad_out):
    local_rows = tokens.shape[0]
    width_rows = weights.shape[0]
    head_width = weights.shape[3]
    head_count = head_width // HD
    dp_devices = lax.axis_size("dp")
    mp_devices = lax.axis_size("mp")
    local_blocks = local_rows // BLOCK
    front_pad = SPAN * local_rows
    window_len = front_pad + local_rows
    my_index = lax.axis_index("dp")
    scale_factor = HD ** (-0.5)
    token_image = jnp.repeat(block_modality, BLOCK) == 1
    my_image = lax.dynamic_slice_in_dim(token_image, my_index * local_rows, local_rows, 0)

    ring = dp_ring(dp_devices)
    inverse = [ring.index(k) for k in range(dp_devices)]
    flat_weights = (
        weights.reshape(width_rows, 2, 3 * head_width)
        .transpose(1, 0, 2)
        .reshape(2 * width_rows, 3 * head_width)
    )
    stacked_weights = lax.all_gather(
        flat_weights, "dp", axis=0, tiled=True, axis_index_groups=[ring]
    )
    columns = lax.all_to_all(tokens, "dp", split_axis=1, concat_axis=0, tiled=True)
    ring_columns = split_by_modality_major(
        ring_blocks(columns, ring, 0), ring_blocks(token_image, ring, 0)
    )
    ring_tokens = ring_blocks(tokens, ring, 1).reshape(local_rows, dp_devices, 1, width_rows)
    ring_tokens = jnp.concatenate(
        [
            jnp.where(my_image[:, None, None, None], jnp.zeros_like(ring_tokens), ring_tokens),
            jnp.where(my_image[:, None, None, None], ring_tokens, jnp.zeros_like(ring_tokens)),
        ],
        axis=2,
    ).reshape(local_rows, -1)
    stacked_weights, ring_columns, ring_tokens = lax.optimization_barrier(
        (stacked_weights, ring_columns, ring_tokens)
    )
    block_weights = stacked_weights.reshape(dp_devices, 2, width_rows, 3 * head_width)

    key_values = (
        jnp.dot(ring_tokens, stacked_weights[:, head_width:], preferred_element_type=jnp.float32)
        .astype(jnp.bfloat16)
        .reshape(local_rows, 2, head_count, HD)
    )
    received = []
    for distance in range(SPAN, 0, -1):
        received.append(shifted(key_values, "dp", distance))
    queries = (
        jnp.dot(ring_tokens, stacked_weights[:, :head_width], preferred_element_type=jnp.float32)
        .astype(jnp.bfloat16)
        .reshape(local_rows, head_count, HD)
    )
    window = jnp.concatenate(received + [key_values], 0)
    key_rows = window[:, 0]
    value_rows = window[:, 1]
    docs_pad = jnp.concatenate([jnp.full((front_pad,), -1, jnp.int32), doc_ids], 0)
    key_docs = lax.dynamic_slice_in_dim(docs_pad, my_index * local_rows, window_len, 0)
    query_docs = lax.dynamic_slice_in_dim(doc_ids, my_index * local_rows, local_rows, 0)
    offsets = jnp.arange(window_len, dtype=jnp.int32) - front_pad
    allowed = (key_docs[None, :] == query_docs[:, None]) & (
        offsets[None, :] <= jnp.arange(local_rows, dtype=jnp.int32)[:, None]
    )
    scores = (
        jnp.einsum("qhd,khd->hqk", queries, key_rows, preferred_element_type=jnp.float32)
        * scale_factor
    )
    scores = jnp.where(allowed[None], scores, -1e30)
    top_score = jnp.max(scores, axis=-1, keepdims=True)
    expos = jnp.where(allowed[None], jnp.exp(scores - top_score), 0.0)
    probs_f = expos / jnp.sum(expos, axis=-1, keepdims=True)
    probs = probs_f.astype(jnp.bfloat16)
    attended = jnp.einsum("hqk,khd->qhd", probs, value_rows, preferred_element_type=jnp.float32)
    attended = attended.astype(jnp.bfloat16).reshape(local_rows, head_width)
    upstream = grad_out.reshape(local_rows, head_count, HD)
    dprob = jnp.einsum("qhd,khd->hqk", upstream, value_rows, preferred_element_type=jnp.float32)
    row_delta = jnp.sum(probs_f * dprob, axis=-1, keepdims=True)
    dscore = (probs_f * (dprob - row_delta)).astype(jnp.bfloat16)
    grad_q = (
        jnp.einsum("hqk,khd->qhd", dscore, key_rows, preferred_element_type=jnp.float32)
        * scale_factor
    )
    grad_k = (
        jnp.einsum("hqk,qhd->khd", dscore, queries, preferred_element_type=jnp.float32)
        * scale_factor
    )
    grad_v = jnp.einsum("hqk,qhd->khd", probs, upstream, preferred_element_type=jnp.float32)
    window_grads = jnp.stack([grad_k, grad_v], 1)
    own_grads = window_grads[front_pad:]
    for distance in range(1, SPAN + 1):
        lower_edge = front_pad - distance * local_rows
        sent_block = window_grads[lower_edge : lower_edge + local_rows]
        own_grads = own_grads + shifted(sent_block.astype(jnp.bfloat16), "dp", -distance).astype(
            sent_block.dtype
        )
    dqkv = (
        jnp.concatenate([grad_q[:, None], own_grads], 1)
        .astype(jnp.bfloat16)
        .reshape(local_rows, 3 * head_width)
    )

    parts = jnp.where(
        my_image[:, None, None],
        lax.dot_general(
            dqkv, block_weights[:, 1], (((1,), (2,)), ((), ())), preferred_element_type=jnp.float32
        ),
        lax.dot_general(
            dqkv, block_weights[:, 0], (((1,), (2,)), ((), ())), preferred_element_type=jnp.float32
        ),
    )
    parts = jnp.take(
        parts.astype(jnp.bfloat16).transpose(1, 0, 2), jnp.array(inverse, jnp.int32), axis=0
    ).reshape(mp_devices, local_rows, -1)
    group_parts = lax.all_to_all(parts, "mp", split_axis=0, concat_axis=0, tiled=True)
    grad_tokens = jnp.sum(group_parts.astype(jnp.float32), axis=0).astype(jnp.bfloat16)

    gathered = lax.all_gather(dqkv, "dp", axis=0, tiled=True, axis_index_groups=[ring])
    weight_sum = lax.dot_general(
        ring_columns,
        gathered,
        (((0,), (0,)), ((), ())),
        preferred_element_type=jnp.float32,
    )
    grad_weights = (
        weight_sum.astype(jnp.bfloat16)
        .reshape(2, width_rows, 3 * head_width)
        .transpose(1, 0, 2)
        .reshape(width_rows, 2, 3, head_width)
    )
    return (attended, grad_tokens, grad_weights)


def solution(mesh):
    return jax.shard_map(
        on_device,
        mesh=mesh,
        in_specs=(P("dp", None), P("dp", None, None, "mp"), P(), P(), P("dp", "mp")),
        out_specs=(P("dp", "mp"), P("dp", "mp"), P("dp", None, None, "mp")),
        check_vma=False,
    )
```

```python
import jax
import jax.numpy as jnp
from jax import lax
from jax.sharding import PartitionSpec as P

HD = 128
BLOCK = 128
SPAN = 4


def shifted(block, axis, distance):
    devices = range(lax.axis_size(axis))
    route = [(i - distance, i) for i in devices if i - distance in devices]
    return lax.ppermute(block, axis, route)


def split_by_modality(rows, is_image):
    zeros = jnp.zeros_like(rows)
    text = jnp.where(is_image[:, None], zeros, rows)
    image = jnp.where(is_image[:, None], rows, zeros)
    return jnp.stack([text, image], axis=2).reshape(rows.shape[0], 2 * rows.shape[1])


def split_by_modality_major(rows, is_image):
    zeros = jnp.zeros_like(rows)
    text = jnp.where(is_image[:, None], zeros, rows)
    image = jnp.where(is_image[:, None], rows, zeros)
    return jnp.concatenate([text, image], axis=1)


def dp_ring(size):
    if size % 4:
        return list(range(size))
    chips = size // 2
    order = [2 * x for x in range(chips // 2)] + [2 * x + 1 for x in reversed(range(chips // 2))]
    return [2 * chip + core for chip in order for core in range(2)]


def ring_blocks(rows, ring, axis):
    shape = rows.shape
    blocks = rows.reshape(shape[:axis] + (len(ring), shape[axis] // len(ring)) + shape[axis + 1 :])
    return jnp.take(blocks, jnp.array(ring, jnp.int32), axis=axis).reshape(shape)


def on_device(tokens, weights, block_modality, doc_ids, grad_out):
    local_rows = tokens.shape[0]
    width_rows = weights.shape[0]
    head_width = weights.shape[3]
    head_count = head_width // HD
    dp_devices = lax.axis_size("dp")
    mp_devices = lax.axis_size("mp")
    local_blocks = local_rows // BLOCK
    front_pad = SPAN * local_rows
    window_len = front_pad + local_rows
    my_index = lax.axis_index("dp")
    scale_factor = HD ** (-0.5)
    token_image = jnp.repeat(block_modality, BLOCK) == 1
    my_image = lax.dynamic_slice_in_dim(token_image, my_index * local_rows, local_rows, 0)

    ring = dp_ring(dp_devices)
    inverse = [ring.index(k) for k in range(dp_devices)]
    flat_weights = (
        weights.reshape(width_rows, 2, 3 * head_width)
        .transpose(1, 0, 2)
        .reshape(2 * width_rows, 3 * head_width)
    )
    stacked_weights = lax.all_gather(
        flat_weights, "dp", axis=0, tiled=True, axis_index_groups=[ring]
    )
    columns = lax.all_to_all(tokens, "dp", split_axis=1, concat_axis=0, tiled=True)
    ring_columns = split_by_modality_major(
        ring_blocks(columns, ring, 0), ring_blocks(token_image, ring, 0)
    )
    ring_tokens = ring_blocks(tokens, ring, 1).reshape(local_rows, dp_devices, 1, width_rows)
    ring_tokens = jnp.concatenate(
        [
            jnp.where(my_image[:, None, None, None], jnp.zeros_like(ring_tokens), ring_tokens),
            jnp.where(my_image[:, None, None, None], ring_tokens, jnp.zeros_like(ring_tokens)),
        ],
        axis=2,
    ).reshape(local_rows, -1)
    stacked_weights, ring_columns, ring_tokens = lax.optimization_barrier(
        (stacked_weights, ring_columns, ring_tokens)
    )
    block_weights = stacked_weights.reshape(dp_devices, 2, width_rows, 3 * head_width)

    key_values = (
        jnp.dot(ring_tokens, stacked_weights[:, head_width:], preferred_element_type=jnp.float32)
        .astype(jnp.bfloat16)
        .reshape(local_rows, 2, head_count, HD)
    )
    received = []
    for distance in range(SPAN, 0, -1):
        received.append(shifted(key_values, "dp", distance))
    queries = (
        jnp.dot(ring_tokens, stacked_weights[:, :head_width], preferred_element_type=jnp.float32)
        .astype(jnp.bfloat16)
        .reshape(local_rows, head_count, HD)
    )
    window = jnp.concatenate(received + [key_values], 0)
    key_rows = window[:, 0]
    value_rows = window[:, 1]
    docs_pad = jnp.concatenate([jnp.full((front_pad,), -1, jnp.int32), doc_ids], 0)
    key_docs = lax.dynamic_slice_in_dim(docs_pad, my_index * local_rows, window_len, 0)
    query_docs = lax.dynamic_slice_in_dim(doc_ids, my_index * local_rows, local_rows, 0)
    offsets = jnp.arange(window_len, dtype=jnp.int32) - front_pad
    allowed = (key_docs[None, :] == query_docs[:, None]) & (
        offsets[None, :] <= jnp.arange(local_rows, dtype=jnp.int32)[:, None]
    )
    scores = (
        jnp.einsum("qhd,khd->hqk", queries, key_rows, preferred_element_type=jnp.float32)
        * scale_factor
    )
    scores = jnp.where(allowed[None], scores, -1e30)
    top_score = jnp.max(scores, axis=-1, keepdims=True)
    expos = jnp.where(allowed[None], jnp.exp(scores - top_score), 0.0)
    probs_f = expos / jnp.sum(expos, axis=-1, keepdims=True)
    probs = probs_f.astype(jnp.bfloat16)
    attended = jnp.einsum("hqk,khd->qhd", probs, value_rows, preferred_element_type=jnp.float32)
    attended = attended.astype(jnp.bfloat16).reshape(local_rows, head_width)
    upstream = grad_out.reshape(local_rows, head_count, HD)
    dprob = jnp.einsum("qhd,khd->hqk", upstream, value_rows, preferred_element_type=jnp.float32)
    row_delta = jnp.sum(probs_f * dprob, axis=-1, keepdims=True)
    dscore = (probs_f * (dprob - row_delta)).astype(jnp.bfloat16)
    grad_q = (
        jnp.einsum("hqk,khd->qhd", dscore, key_rows, preferred_element_type=jnp.float32)
        * scale_factor
    )
    grad_k = (
        jnp.einsum("hqk,qhd->khd", dscore, queries, preferred_element_type=jnp.float32)
        * scale_factor
    )
    grad_v = jnp.einsum("hqk,qhd->khd", probs, upstream, preferred_element_type=jnp.float32)
    window_grads = jnp.stack([grad_k, grad_v], 1)
    own_grads = window_grads[front_pad:]
    for distance in range(1, SPAN + 1):
        lower_edge = front_pad - distance * local_rows
        sent_block = window_grads[lower_edge : lower_edge + local_rows]
        own_grads = own_grads + shifted(sent_block.astype(jnp.bfloat16), "dp", -distance).astype(
            sent_block.dtype
        )
    dqkv = (
        jnp.concatenate([grad_q[:, None], own_grads], 1)
        .astype(jnp.bfloat16)
        .reshape(local_rows, 3 * head_width)
    )

    zeros = jnp.zeros_like(dqkv)
    parts = lax.dot_general(
        jnp.where(my_image[:, None], zeros, dqkv),
        block_weights[:, 0],
        (((1,), (2,)), ((), ())),
        preferred_element_type=jnp.float32,
    ) + lax.dot_general(
        jnp.where(my_image[:, None], dqkv, zeros),
        block_weights[:, 1],
        (((1,), (2,)), ((), ())),
        preferred_element_type=jnp.float32,
    )
    parts = jnp.take(
        parts.astype(jnp.bfloat16).transpose(1, 0, 2), jnp.array(inverse, jnp.int32), axis=0
    ).reshape(mp_devices, local_rows, -1)
    group_parts = lax.all_to_all(parts, "mp", split_axis=0, concat_axis=0, tiled=True)
    grad_tokens = jnp.sum(group_parts.astype(jnp.float32), axis=0).astype(jnp.bfloat16)

    gathered = lax.all_gather(dqkv[None], "dp", axis=0, tiled=True, axis_index_groups=[ring])
    weight_sum = lax.dot_general(
        ring_columns.reshape(dp_devices, local_rows, -1),
        gathered,
        (((0, 1), (0, 1)), ((), ())),
        preferred_element_type=jnp.float32,
    )
    grad_weights = (
        weight_sum.astype(jnp.bfloat16)
        .reshape(2, width_rows, 3 * head_width)
        .transpose(1, 0, 2)
        .reshape(width_rows, 2, 3, head_width)
    )
    return (attended, grad_tokens, grad_weights)


def solution(mesh):
    return jax.shard_map(
        on_device,
        mesh=mesh,
        in_specs=(P("dp", None), P("dp", None, None, "mp"), P(), P(), P("dp", "mp")),
        out_specs=(P("dp", "mp"), P("dp", "mp"), P("dp", None, None, "mp")),
        check_vma=False,
    )
```

```python
import jax
import jax.numpy as jnp
from jax import lax
from jax.sharding import PartitionSpec as P

HD = 128
BLOCK = 128
SPAN = 4


def shifted(block, axis, distance):
    devices = range(lax.axis_size(axis))
    route = [(i - distance, i) for i in devices if i - distance in devices]
    return lax.ppermute(block, axis, route)


def split_by_modality(rows, is_image):
    zeros = jnp.zeros_like(rows)
    text = jnp.where(is_image[:, None], zeros, rows)
    image = jnp.where(is_image[:, None], rows, zeros)
    return jnp.stack([text, image], axis=2).reshape(rows.shape[0], 2 * rows.shape[1])


def split_by_modality_major(rows, is_image):
    zeros = jnp.zeros_like(rows)
    text = jnp.where(is_image[:, None], zeros, rows)
    image = jnp.where(is_image[:, None], rows, zeros)
    return jnp.concatenate([text, image], axis=1)


def dp_ring(size):
    if size % 4:
        return list(range(size))
    chips = size // 2
    order = [2 * x for x in range(chips // 2)] + [2 * x + 1 for x in reversed(range(chips // 2))]
    return [2 * chip + core for chip in order for core in range(2)]


def ring_blocks(rows, ring, axis):
    shape = rows.shape
    blocks = rows.reshape(shape[:axis] + (len(ring), shape[axis] // len(ring)) + shape[axis + 1 :])
    return jnp.take(blocks, jnp.array(ring, jnp.int32), axis=axis).reshape(shape)


def on_device(tokens, weights, block_modality, doc_ids, grad_out):
    local_rows = tokens.shape[0]
    width_rows = weights.shape[0]
    head_width = weights.shape[3]
    head_count = head_width // HD
    dp_devices = lax.axis_size("dp")
    mp_devices = lax.axis_size("mp")
    local_blocks = local_rows // BLOCK
    front_pad = SPAN * local_rows
    window_len = front_pad + local_rows
    my_index = lax.axis_index("dp")
    scale_factor = HD ** (-0.5)
    token_image = jnp.repeat(block_modality, BLOCK) == 1
    my_image = lax.dynamic_slice_in_dim(token_image, my_index * local_rows, local_rows, 0)

    ring = dp_ring(dp_devices)
    inverse = [ring.index(k) for k in range(dp_devices)]
    flat_weights = (
        weights.reshape(width_rows, 2, 3 * head_width)
        .transpose(1, 0, 2)
        .reshape(2 * width_rows, 3 * head_width)
    )
    stacked_weights = lax.all_gather(
        flat_weights, "dp", axis=0, tiled=True, axis_index_groups=[ring]
    )
    columns = lax.all_to_all(tokens, "dp", split_axis=1, concat_axis=0, tiled=True)
    ring_columns = split_by_modality_major(
        ring_blocks(columns, ring, 0), ring_blocks(token_image, ring, 0)
    )
    ring_tokens = ring_blocks(tokens, ring, 1).reshape(local_rows, dp_devices, 1, width_rows)
    ring_tokens = jnp.concatenate(
        [
            jnp.where(my_image[:, None, None, None], jnp.zeros_like(ring_tokens), ring_tokens),
            jnp.where(my_image[:, None, None, None], ring_tokens, jnp.zeros_like(ring_tokens)),
        ],
        axis=2,
    ).reshape(local_rows, -1)
    stacked_weights, ring_columns, ring_tokens = lax.optimization_barrier(
        (stacked_weights, ring_columns, ring_tokens)
    )
    block_weights = stacked_weights.reshape(dp_devices, 2, width_rows, 3 * head_width)

    key_values = (
        jnp.dot(ring_tokens, stacked_weights[:, head_width:], preferred_element_type=jnp.float32)
        .astype(jnp.bfloat16)
        .reshape(local_rows, 2, head_count, HD)
    )
    received = []
    for distance in range(SPAN, 0, -1):
        received.append(shifted(key_values, "dp", distance))
    queries = (
        jnp.dot(ring_tokens, stacked_weights[:, :head_width], preferred_element_type=jnp.float32)
        .astype(jnp.bfloat16)
        .reshape(local_rows, head_count, HD)
    )
    window = jnp.concatenate(received + [key_values], 0)
    key_rows = window[:, 0]
    value_rows = window[:, 1]
    docs_pad = jnp.concatenate([jnp.full((front_pad,), -1, jnp.int32), doc_ids], 0)
    key_docs = lax.dynamic_slice_in_dim(docs_pad, my_index * local_rows, window_len, 0)
    query_docs = lax.dynamic_slice_in_dim(doc_ids, my_index * local_rows, local_rows, 0)
    offsets = jnp.arange(window_len, dtype=jnp.int32) - front_pad
    allowed = (key_docs[None, :] == query_docs[:, None]) & (
        offsets[None, :] <= jnp.arange(local_rows, dtype=jnp.int32)[:, None]
    )
    scores = (
        jnp.einsum("qhd,khd->hqk", queries, key_rows, preferred_element_type=jnp.float32)
        * scale_factor
    )
    scores = jnp.where(allowed[None], scores, -1e30)
    top_score = jnp.max(scores, axis=-1, keepdims=True)
    expos = jnp.where(allowed[None], jnp.exp(scores - top_score), 0.0)
    probs_f = expos / jnp.sum(expos, axis=-1, keepdims=True)
    probs = probs_f.astype(jnp.bfloat16)
    attended = jnp.einsum("hqk,khd->qhd", probs, value_rows, preferred_element_type=jnp.float32)
    attended = attended.astype(jnp.bfloat16).reshape(local_rows, head_width)
    upstream = grad_out.reshape(local_rows, head_count, HD)
    dprob = jnp.einsum("qhd,khd->hqk", upstream, value_rows, preferred_element_type=jnp.float32)
    row_delta = jnp.sum(probs_f * dprob, axis=-1, keepdims=True)
    dscore = (probs_f * (dprob - row_delta)).astype(jnp.bfloat16)
    grad_q = (
        jnp.einsum("hqk,khd->qhd", dscore, key_rows, preferred_element_type=jnp.float32)
        * scale_factor
    )
    blocks = (head_count, local_rows, SPAN + 1, local_rows)
    grad_k = (
        jnp.einsum(
            "hqbk,qhd->bkhd", dscore.reshape(blocks), queries, preferred_element_type=jnp.float32
        )
        * scale_factor
    )
    grad_v = jnp.einsum(
        "hqbk,qhd->bkhd", probs.reshape(blocks), upstream, preferred_element_type=jnp.float32
    )
    window_grads = jnp.stack([grad_k, grad_v], 2)
    own_grads = window_grads[SPAN]
    for distance in range(1, SPAN + 1):
        sent_block = window_grads[SPAN - distance]
        own_grads = own_grads + shifted(sent_block.astype(jnp.bfloat16), "dp", -distance).astype(
            sent_block.dtype
        )
    dqkv = (
        jnp.concatenate([grad_q[:, None], own_grads], 1)
        .astype(jnp.bfloat16)
        .reshape(local_rows, 3 * head_width)
    )

    zeros = jnp.zeros_like(dqkv)
    parts = lax.dot_general(
        jnp.where(my_image[:, None], zeros, dqkv),
        block_weights[:, 0],
        (((1,), (2,)), ((), ())),
        preferred_element_type=jnp.float32,
    ) + lax.dot_general(
        jnp.where(my_image[:, None], dqkv, zeros),
        block_weights[:, 1],
        (((1,), (2,)), ((), ())),
        preferred_element_type=jnp.float32,
    )
    parts = jnp.take(
        parts.astype(jnp.bfloat16).transpose(1, 0, 2), jnp.array(inverse, jnp.int32), axis=0
    ).reshape(mp_devices, local_rows, -1)
    group_parts = lax.all_to_all(parts, "mp", split_axis=0, concat_axis=0, tiled=True)
    grad_tokens = jnp.sum(group_parts.astype(jnp.float32), axis=0).astype(jnp.bfloat16)

    gathered = lax.all_gather(dqkv[None], "dp", axis=0, tiled=True, axis_index_groups=[ring])
    weight_sum = lax.dot_general(
        ring_columns.reshape(dp_devices, local_rows, -1),
        gathered,
        (((0, 1), (0, 1)), ((), ())),
        preferred_element_type=jnp.float32,
    )
    grad_weights = (
        weight_sum.astype(jnp.bfloat16)
        .reshape(2, width_rows, 3 * head_width)
        .transpose(1, 0, 2)
        .reshape(width_rows, 2, 3, head_width)
    )
    return (attended, grad_tokens, grad_weights)


def solution(mesh):
    return jax.shard_map(
        on_device,
        mesh=mesh,
        in_specs=(P("dp", None), P("dp", None, None, "mp"), P(), P(), P("dp", "mp")),
        out_specs=(P("dp", "mp"), P("dp", "mp"), P("dp", None, None, "mp")),
        check_vma=False,
    )
```
